32 devices in a mesh: ctx: 8 (over y, x, core), head: 4 (over z).
Axes of the slice: x: 2, y: 2, z: 4, core: 2. Of those that a mesh axis runs over, the one named last changes fastest.
Arguments:
- query_rows: bfloat16 [6144, 4096], P('ctx', 'head'), may hold values from -6 to 6
- key_rows: bfloat16 [6144, 4096], P('ctx', 'head'), may hold values from -3.5 to 3.5
- value_rows: bfloat16 [6144, 4096], P('ctx', 'head'), may hold values from -6 to 6
- cluster_ids: int32 [32, 6144, 1], P('head', 'ctx'), may hold values from 0 to 255; in each aligned block of 768 rows (0 to 767, 768 to 1535, ..., all dimensions but the last counted through in order) at most 6 rows name the same one
- centroids: float32 [32, 256, 128], P('head', 'ctx'), may hold values from -6 to 6
- out_weight: bfloat16 [4096, 4096], P(None, 'head'), may hold values from -0.09375 to 0.09375
Outputs:
- layer_output: bfloat16 [6144, 4096], P('ctx', 'head')
- new_centroids: float32 [32, 256, 128], P('head', 'ctx')
The draws below stay inside these ranges and needn't reach their ends.
Inputs may be any that keep to these rules, and one draw needn't show every extreme that they name: `cluster_ids`: in each aligned block of 768 tokens of one head (the tokens of one index of ctx), no cluster is named by more than 6 tokens, a bound that some block reaches.
All inputs are finite; a program needn't handle non-finite values.
Results may differ from the reference program's by a relative error of at most 0.014.
Values may be sent and summed in bfloat16 or wider, within the bound.
No kernel may reach another device: no remote copies, remote signals or barrier semaphores. Data moves between devices by JAX's collectives and lax.ppermute only.
A program may use at most 128 MiB of HBM per device.

```python
import math
import jax
import jax.numpy as jnp
import numpy as np
from jax import lax

D = 4096
HEADS = 32
HD = 128
CLUSTERS = 256
TOK_DEV = 768
SLOT = 6
TOKENS = 6144
N_CTX = 8


def shared_rows(key):
    base = jax.random.fold_in(key, 7)
    key_query, key_other = jax.random.split(base, 2)
    shape_rows = (TOKENS, HEADS * HD)
    query_base = jnp.clip(jax.random.normal(key_query, shape_rows, jnp.float32), -3.5, 3.5)
    key_base = jnp.clip(jax.random.normal(key_other, shape_rows, jnp.float32), -3.5, 3.5)
    return (query_base, key_base)


def draw_query_rows(key, part):
    return shared_rows(key)[0].astype(jnp.bfloat16)


def draw_key_rows(key, part):
    return shared_rows(key)[1].astype(jnp.bfloat16)


def block_levels(rng, shape, cuts, low, high):
    def one(dim, blocks):
        steps = jax.random.uniform(jax.random.fold_in(jax.random.fold_in(rng, 6), dim), (blocks,), jnp.float32, low / len(cuts), high / len(cuts))
        return jnp.repeat(jnp.exp(steps), shape[dim] // blocks).reshape((-1,) + (1,) * (len(shape) - dim - 1))

    level = one(*cuts[0])
    for cut in cuts[1:]:
        level = level * one(*cut)
    return level


def routed_block(stream_key, own, number, rows, amount, top, most, skew):
    ranking = jax.random.permutation(stream_key, amount)
    crowded, ordinary = portions_of(amount, rows * top, most, skew, True), portions_of(amount, rows * top, most, skew, False)
    places = jnp.arange(amount)

    def named(lengths, rotation):
        used = int((lengths > 0).sum())
        fixed = max(1, used // 4)
        moved = fixed + (places - fixed + rotation * (used - fixed)) % max(1, amount - fixed)
        return jnp.zeros((amount,), jnp.int32).at[ranking[jnp.where(places < fixed, places, moved)]].set(jnp.asarray(lengths, jnp.int32))

    lengths = jnp.where(number % 4 == 0, named(crowded, number // 4), named(ordinary, number - number // 4 - 1))
    mixed = jax.random.permutation(jax.random.fold_in(own, 3), amount)
    donor, receiver = mixed[0:amount // 2 * 2:2], mixed[1:amount // 2 * 2:2]
    room = jnp.minimum(lengths[donor] - 1, most - lengths[receiver]) // 2
    room = jnp.where((donor == ranking[0]) | (receiver == ranking[0]) | (lengths[receiver] == 0), 0, jnp.maximum(room, 0))
    moved = jax.random.randint(jax.random.fold_in(own, 4), (amount // 2,), 0, 1 << 20) % (room + 1)
    lengths = lengths.at[donor].add(-moved).at[receiver].add(moved)
    items = jnp.searchsorted(jnp.cumsum(lengths), jnp.arange(rows * top), side="right").astype(jnp.int32)
    grid = items.reshape(top, rows).T
    grid = grid[jax.random.permutation(jax.random.fold_in(own, 1), rows)]
    rotation = jax.random.randint(jax.random.fold_in(own, 2), (rows, 1), 0, top)
    return jnp.take_along_axis(grid, (jnp.arange(top)[None, :] + rotation) % top, axis=1)


def portions_of(amount, total, reach, slope, full):
    loads = [(1 << 20) // math.isqrt(grade ** slope) + 1 for grade in range(1, amount + 1)]
    largest = reach if full else min(reach, max(-(-total // amount), total * loads[0] // sum(loads)))
    least = 1 if total - largest >= amount - 1 else 0
    holding, spare = [largest] + [least] * (amount - 1), total - largest - least * (amount - 1)
    while spare > 0:
        free = [i for i in range(1, amount) if holding[i] < largest] or [i for i in range(1, amount) if holding[i] < reach]
        whole, budget = sum([loads[i] for i in free]), spare
        for i in free:
            addition = min(reach - holding[i], max(1, budget * loads[i] // whole), spare)
            holding[i] = holding[i] + addition
            spare = spare - addition
    return np.array(holding)


def noise(key, extent, width, reach, cuts=(), held_as=jnp.bfloat16):
    loudness = block_levels(key, extent, cuts, -0.22, 0.18) if cuts else 1.0
    array = jax.random.normal(key, extent, jnp.float32) * width * loudness
    return jnp.minimum(jnp.maximum(array, -reach), reach).astype(held_as)


def setup_inputs(seed: int = 0) -> dict:
    keys = jax.random.split(jax.random.key(seed), 7)
    query_rows = draw_query_rows(jax.random.fold_in(keys[6], 71), 0)
    key_rows = draw_key_rows(jax.random.fold_in(keys[6], 71), 0)
    value_rows = noise(keys[2], (TOKENS, HEADS * HD), 1.0, 6.0, ((0, 8), (1, 4)))
    cluster_ids_keys = jax.random.split(jax.random.fold_in(keys[3], 1), HEADS * TOKENS // TOK_DEV)
    cluster_ids_turns = jax.random.permutation(jax.random.fold_in(keys[3], 3), HEADS * TOKENS // TOK_DEV)
    cluster_ids = jax.vmap(lambda own, number: routed_block(jax.random.fold_in(keys[3], 2), own, number, TOK_DEV, CLUSTERS, 1, SLOT, 2))(cluster_ids_keys, cluster_ids_turns).reshape((HEADS, TOKENS, 1))
    centroids = noise(keys[4], (HEADS, CLUSTERS, HD), 1.0, 6.0, ((0, 4), (1, 8)), jnp.float32)
    out_weight = noise(keys[5], (HEADS * HD, D), (HEADS * HD) ** -0.5, 0.09375, ((1, 4),))
    return {"query_rows": query_rows, "key_rows": key_rows, "value_rows": value_rows, "cluster_ids": cluster_ids, "centroids": centroids, "out_weight": out_weight}


prior_weight = 64.0


def cluster_head(query_col, key_col, value_col, labels):
    length = labels.shape[0]
    group = N_CTX * SLOT
    ordering = jnp.argsort(labels, stable=True).astype(jnp.int32)
    counts = jnp.sum((labels[:, None] == jnp.arange(CLUSTERS, dtype=jnp.int32)[None, :]).astype(jnp.int32), axis=0)
    starts = jnp.cumsum(counts) - counts
    sorted_labels = labels[ordering]
    slot_index = (sorted_labels * group + (jnp.arange(length, dtype=jnp.int32) - starts[sorted_labels])).astype(jnp.int32)

    def spread(source):
        filled = jnp.zeros((CLUSTERS * group, HD), source.dtype).at[slot_index].set(source[ordering])
        return filled.reshape(CLUSTERS, group, HD)

    query_buf = spread(query_col)
    key_buf = spread(key_col)
    value_buf = spread(value_col)
    place_buf = jnp.full((CLUSTERS * group,), -1, jnp.int32).at[slot_index].set(ordering).reshape(CLUSTERS, group)
    scores = jnp.einsum("cid,cjd->cij", query_buf.astype(jnp.float32), key_buf.astype(jnp.float32)) * (HD ** -0.5)
    allowed = (place_buf[:, None, :] >= 0) & (place_buf[:, None, :] <= place_buf[:, :, None])
    scores = jnp.where(allowed, scores, jnp.float32(-1e30))
    top_score = jnp.max(scores, axis=2, keepdims=True)
    weights = jnp.exp(scores - top_score)
    totals = jnp.sum(weights, axis=2, keepdims=True)
    attention_weights = (weights / totals).astype(jnp.bfloat16)
    result = jnp.einsum("cij,cjd->cid", attention_weights.astype(jnp.float32), value_buf.astype(jnp.float32)).astype(jnp.bfloat16)
    flat_result = result.reshape(CLUSTERS * group, HD)
    out_tokens = jnp.zeros((length, HD), jnp.bfloat16).at[ordering].set(flat_result[slot_index])
    key_sums = jnp.sum(key_buf.astype(jnp.float32), axis=1)
    key_counts = counts.astype(jnp.float32)
    return out_tokens, key_sums, key_counts


def reference(query_rows, key_rows, value_rows, cluster_ids, centroids, out_weight):
    length = query_rows.shape[0]

    def per_head(head_number):
        first_col = head_number * HD
        query_col = lax.dynamic_slice_in_dim(query_rows, first_col, HD, 1)
        key_col = lax.dynamic_slice_in_dim(key_rows, first_col, HD, 1)
        value_col = lax.dynamic_slice_in_dim(value_rows, first_col, HD, 1)
        labels = lax.dynamic_index_in_dim(cluster_ids, head_number, 0, keepdims=False)[:, 0]
        return cluster_head(query_col, key_col, value_col, labels)

    head_results, key_sums, key_counts = lax.map(per_head, jnp.arange(HEADS, dtype=jnp.int32))
    attended = jnp.transpose(head_results, (1, 0, 2)).reshape(length, HEADS * HD)
    layer_output = jnp.dot(attended, out_weight, preferred_element_type=jnp.float32).astype(jnp.bfloat16)
    new_centroids = (prior_weight * centroids + key_sums) / (prior_weight + key_counts[:, :, None])
    return layer_output, new_centroids
```

```python
import jax
import jax.numpy as jnp
from jax import lax
from jax.sharding import PartitionSpec as P

CLUSTERS = 256


prior_weight = 64.0


def slot_targets(labels, per_owner, slot_count):
    length = labels.shape[1]
    order_ids = jnp.arange(length, dtype=jnp.int32)
    same_label = labels[:, :, None] == labels[:, None, :]
    earlier = order_ids[None, :] < order_ids[:, None]
    token_rank = jnp.sum((same_label & earlier[None]).astype(jnp.int32), axis=2)
    owner_of = labels // per_owner
    local_of = labels % per_owner
    return owner_of * (slot_count * per_owner) + token_rank * per_owner + local_of


def attend_blocks(recv, counts_recv, per_owner, head_dim):
    heads_here, sources, width_slots, _ = recv.shape
    slot_count = width_slots // per_owner
    row_count = sources * slot_count
    view = recv.reshape(heads_here, row_count, per_owner, 3 * head_dim)
    query_view = view[..., :head_dim]
    key_view = view[..., head_dim : 2 * head_dim]
    value_view = view[..., 2 * head_dim :]
    rank_ids = jnp.arange(slot_count, dtype=jnp.int32)
    valid = rank_ids[None, None, :, None] < counts_recv[:, :, None, :]
    valid = jnp.transpose(valid.reshape(heads_here, row_count, per_owner), (0, 2, 1))
    row_ids = jnp.arange(row_count, dtype=jnp.int32)
    causal = row_ids[None, :] <= row_ids[:, None]
    allowed = valid[:, :, None, :] & causal[None, None]
    scores = jnp.einsum(
        "hicd,hjcd->hcij", query_view, key_view, preferred_element_type=jnp.float32
    ) * head_dim ** (-0.5)
    scores = jnp.where(allowed, scores, jnp.float32(-1e30))
    top_score = jnp.max(scores, axis=3, keepdims=True)
    weights = jnp.exp(scores - top_score)
    totals = jnp.sum(weights, axis=3, keepdims=True)
    attention_weights = (weights / totals).astype(jnp.bfloat16)
    result = jnp.einsum(
        "hcij,hjcd->hicd", attention_weights, value_view, preferred_element_type=jnp.float32
    ).astype(jnp.bfloat16)
    key_sums = jnp.sum(key_view.astype(jnp.float32), axis=1)
    key_counts = jnp.sum(counts_recv, axis=1).astype(jnp.float32)
    return result.reshape(heads_here, sources, width_slots, head_dim), key_sums, key_counts


def local(query_rows, key_rows, value_rows, cluster_ids, centroids, out_weight):
    ctx_count = lax.axis_size("ctx")
    token_count = query_rows.shape[0]
    heads_here = cluster_ids.shape[0]
    head_dim = query_rows.shape[1] // heads_here
    clusters = CLUSTERS
    per_owner = clusters // ctx_count
    slot_count = 2 * token_count // clusters
    row_total = clusters * slot_count
    labels = cluster_ids[:, :, 0]
    targets = slot_targets(labels, per_owner, slot_count)
    head_ids = jnp.arange(heads_here, dtype=jnp.int32)
    token_ids = jnp.arange(token_count, dtype=jnp.int32)
    token_at = jnp.full((heads_here, row_total), token_count, jnp.int32)
    token_at = token_at.at[head_ids[:, None], targets].set(
        jnp.broadcast_to(token_ids[None, :], targets.shape), unique_indices=True
    )
    filled_slot = token_at < token_count
    flat_index = jnp.where(filled_slot, token_at * heads_here + head_ids[:, None], 0)

    def pick(rows):
        table = rows.reshape(token_count * heads_here, head_dim)
        got = jnp.take(table, flat_index, axis=0)
        return jnp.where(filled_slot[..., None], got, jnp.zeros_like(got))

    send = jnp.concatenate(
        (pick(query_rows), pick(key_rows), pick(value_rows)), axis=2
    ).reshape(heads_here, ctx_count, slot_count * per_owner, 3 * head_dim)
    one_hot = labels[:, :, None] == jnp.arange(clusters, dtype=jnp.int32)[None, None, :]
    counts_send = jnp.sum(one_hot.astype(jnp.int32), axis=1).reshape(
        heads_here, ctx_count, per_owner
    )
    recv = lax.all_to_all(send, "ctx", split_axis=1, concat_axis=1, tiled=True)
    counts_recv = lax.all_to_all(counts_send, "ctx", split_axis=1, concat_axis=1, tiled=True)
    result, key_sums, key_counts = attend_blocks(recv, counts_recv, per_owner, head_dim)
    new_centroids = (prior_weight * centroids + key_sums) / (prior_weight + key_counts[:, :, None])
    returned = lax.all_to_all(result, "ctx", split_axis=1, concat_axis=1, tiled=True)
    returned_flat = returned.reshape(heads_here * row_total, head_dim)
    back_index = jnp.transpose(targets + head_ids[:, None] * row_total, (1, 0))
    attended = jnp.take(returned_flat, back_index, axis=0).reshape(
        token_count, heads_here * head_dim
    )
    mixed_total = jnp.dot(
        lax.all_gather(attended, "head", axis=1, tiled=True),
        out_weight,
        preferred_element_type=jnp.float32,
    )
    return (mixed_total.astype(jnp.bfloat16), new_centroids)


def solution(mesh):
    placed = (
        P("ctx", "head"),
        P("ctx", "head"),
        P("ctx", "head"),
        P("head", "ctx", None),
        P("head", "ctx", None),
        P(None, "head"),
    )
    return jax.shard_map(
        local,
        mesh=mesh,
        in_specs=placed,
        out_specs=(P("ctx", "head"), P("head", "ctx", None)),
        check_vma=False,
    )
```

```python
import jax
import jax.numpy as jnp
from jax import lax
from jax.sharding import PartitionSpec as P

CLUSTERS = 256


prior_weight = 64.0


def slot_targets(labels, per_owner, slot_count):
    length = labels.shape[1]
    order_ids = jnp.arange(length, dtype=jnp.int32)
    same_label = labels[:, :, None] == labels[:, None, :]
    earlier = order_ids[None, :] < order_ids[:, None]
    token_rank = jnp.sum((same_label & earlier[None]).astype(jnp.int32), axis=2)
    owner_of = labels // per_owner
    local_of = labels % per_owner
    return owner_of * (slot_count * per_owner) + token_rank * per_owner + local_of


def attend_blocks(recv, counts_recv, per_owner, head_dim):
    heads_here, sources, width_slots, _ = recv.shape
    slot_count = width_slots // per_owner
    row_count = sources * slot_count
    view = recv.reshape(heads_here, row_count, per_owner, 3 * head_dim)
    query_view = view[..., :head_dim]
    key_view = view[..., head_dim : 2 * head_dim]
    value_view = view[..., 2 * head_dim :]
    rank_ids = jnp.arange(slot_count, dtype=jnp.int32)
    valid = rank_ids[None, None, :, None] < counts_recv[:, :, None, :]
    valid = jnp.transpose(valid.reshape(heads_here, row_count, per_owner), (0, 2, 1))
    row_ids = jnp.arange(row_count, dtype=jnp.int32)
    causal = row_ids[None, :] <= row_ids[:, None]
    allowed = valid[:, :, None, :] & causal[None, None]
    scores = jnp.einsum(
        "hicd,hjcd->hcij", query_view, key_view, preferred_element_type=jnp.float32
    ) * head_dim ** (-0.5)
    scores = jnp.where(allowed, scores, jnp.float32(-1e30))
    top_score = jnp.max(scores, axis=3, keepdims=True)
    weights = jnp.exp(scores - top_score)
    totals = jnp.sum(weights, axis=3, keepdims=True)
    attention_weights = (weights / totals).astype(jnp.bfloat16)
    result = jnp.einsum(
        "hcij,hjcd->hicd", attention_weights, value_view, preferred_element_type=jnp.float32
    ).astype(jnp.bfloat16)
    key_sums = jnp.sum(key_view.astype(jnp.float32), axis=1)
    key_counts = jnp.sum(counts_recv, axis=1).astype(jnp.float32)
    return result.reshape(heads_here, sources, width_slots, head_dim), key_sums, key_counts


GROUPS = 2


def local(query_rows, key_rows, value_rows, cluster_ids, centroids, out_weight):
    ctx_count = lax.axis_size("ctx")
    head_count = lax.axis_size("head")
    token_count = query_rows.shape[0]
    heads_here = cluster_ids.shape[0]
    head_dim = query_rows.shape[1] // heads_here
    out_cols = out_weight.shape[1]
    clusters = CLUSTERS
    per_owner = clusters // ctx_count
    slot_count = 2 * token_count // clusters
    row_total = clusters * slot_count
    groups = GROUPS if heads_here % GROUPS == 0 else 1
    group_heads = heads_here // groups
    labels = cluster_ids[:, :, 0]
    targets = slot_targets(labels, per_owner, slot_count)
    one_hot = labels[:, :, None] == jnp.arange(clusters, dtype=jnp.int32)[None, None, :]
    counts_send = jnp.sum(one_hot.astype(jnp.int32), axis=1).reshape(
        heads_here, ctx_count, per_owner
    )
    counts_recv = lax.all_to_all(counts_send, "ctx", split_axis=1, concat_axis=1, tiled=True)
    stacked = jnp.concatenate(
        (
            query_rows.reshape(token_count, heads_here, head_dim),
            key_rows.reshape(token_count, heads_here, head_dim),
            value_rows.reshape(token_count, heads_here, head_dim),
        ),
        axis=2,
    )
    weight_view = out_weight.reshape(head_count, groups, group_heads * head_dim, out_cols)
    slot_ids = jnp.arange(row_total, dtype=jnp.int32)
    mixed_total = None
    sums_parts, counts_parts = [], []
    for g in range(groups):
        heads = slice(g * group_heads, (g + 1) * group_heads)
        selector = (slot_ids[None, :, None] == targets[heads][:, None, :]).astype(jnp.bfloat16)
        send = jnp.einsum(
            "hrt,thd->hrd", selector, stacked[:, heads], preferred_element_type=jnp.float32
        ).astype(jnp.bfloat16)
        send = send.reshape(group_heads, ctx_count, slot_count * per_owner, 3 * head_dim)
        recv = lax.all_to_all(send, "ctx", split_axis=1, concat_axis=1, tiled=True)
        result, key_sums, key_counts = attend_blocks(recv, counts_recv[heads], per_owner, head_dim)
        sums_parts.append(key_sums)
        counts_parts.append(key_counts)
        returned = lax.all_to_all(result, "ctx", split_axis=1, concat_axis=1, tiled=True)
        returned = returned.reshape(group_heads, row_total, head_dim)
        attended = jnp.einsum(
            "hrt,hrd->thd", selector, returned, preferred_element_type=jnp.float32
        ).astype(jnp.bfloat16).reshape(token_count, group_heads * head_dim)
        gathered = lax.all_gather(attended, "head", axis=1, tiled=True)
        part = jnp.dot(
            gathered,
            weight_view[:, g].reshape(head_count * group_heads * head_dim, out_cols),
            preferred_element_type=jnp.float32,
        )
        mixed_total = part if mixed_total is None else mixed_total + part
    key_sums = jnp.concatenate(sums_parts, axis=0)
    key_counts = jnp.concatenate(counts_parts, axis=0)
    new_centroids = (prior_weight * centroids + key_sums) / (prior_weight + key_counts[:, :, None])
    return (mixed_total.astype(jnp.bfloat16), new_centroids)


def solution(mesh):
    placed = (
        P("ctx", "head"),
        P("ctx", "head"),
        P("ctx", "head"),
        P("head", "ctx", None),
        P("head", "ctx", None),
        P(None, "head"),
    )
    return jax.shard_map(
        local,
        mesh=mesh,
        in_specs=placed,
        out_specs=(P("ctx", "head"), P("head", "ctx", None)),
        check_vma=False,
    )
```

```python
import jax
import jax.numpy as jnp
from jax import lax
from jax.sharding import PartitionSpec as P

CLUSTERS = 256


prior_weight = 64.0


def slot_targets(labels, per_owner, slot_count):
    length = labels.shape[1]
    order_ids = jnp.arange(length, dtype=jnp.int32)
    same_label = labels[:, :, None] == labels[:, None, :]
    earlier = order_ids[None, :] < order_ids[:, None]
    token_rank = jnp.sum((same_label & earlier[None]).astype(jnp.int32), axis=2)
    owner_of = labels // per_owner
    local_of = labels % per_owner
    return owner_of * (slot_count * per_owner) + token_rank * per_owner + local_of


def attend_blocks(recv, counts_recv, per_owner, head_dim):
    heads_here, sources, width_slots, _ = recv.shape
    slot_count = width_slots // per_owner
    row_count = sources * slot_count
    view = recv.reshape(heads_here, row_count, per_owner, 3 * head_dim)
    query_view = view[..., :head_dim]
    key_view = view[..., head_dim : 2 * head_dim]
    value_view = view[..., 2 * head_dim :]
    rank_ids = jnp.arange(slot_count, dtype=jnp.int32)
    valid = rank_ids[None, None, :, None] < counts_recv[:, :, None, :]
    valid = jnp.transpose(valid.reshape(heads_here, row_count, per_owner), (0, 2, 1))
    row_ids = jnp.arange(row_count, dtype=jnp.int32)
    causal = row_ids[None, :] <= row_ids[:, None]
    allowed = valid[:, :, None, :] & causal[None, None]
    scores = jnp.einsum(
        "hicd,hjcd->hcij", query_view, key_view, preferred_element_type=jnp.float32
    ) * head_dim ** (-0.5)
    scores = jnp.where(allowed, scores, jnp.float32(-1e30))
    top_score = jnp.max(scores, axis=3, keepdims=True)
    weights = jnp.exp(scores - top_score)
    totals = jnp.sum(weights, axis=3, keepdims=True)
    attention_weights = (weights / totals).astype(jnp.bfloat16)
    result = jnp.einsum(
        "hcij,hjcd->hicd", attention_weights, value_view, preferred_element_type=jnp.float32
    ).astype(jnp.bfloat16)
    key_sums = jnp.sum(key_view.astype(jnp.float32), axis=1)
    key_counts = jnp.sum(counts_recv, axis=1).astype(jnp.float32)
    return result.reshape(heads_here, sources, width_slots, head_dim), key_sums, key_counts


GROUP_SIZES = (3, 3, 2)


def local(query_rows, key_rows, value_rows, cluster_ids, centroids, out_weight):
    ctx_count = lax.axis_size("ctx")
    head_count = lax.axis_size("head")
    token_count = query_rows.shape[0]
    heads_here = cluster_ids.shape[0]
    head_dim = query_rows.shape[1] // heads_here
    out_cols = out_weight.shape[1]
    clusters = CLUSTERS
    per_owner = clusters // ctx_count
    slot_count = 2 * token_count // clusters
    row_total = clusters * slot_count
    sizes = GROUP_SIZES if sum(GROUP_SIZES) == heads_here else (heads_here,)
    labels = cluster_ids[:, :, 0]
    targets = slot_targets(labels, per_owner, slot_count)
    one_hot = labels[:, :, None] == jnp.arange(clusters, dtype=jnp.int32)[None, None, :]
    counts_send = jnp.sum(one_hot.astype(jnp.int32), axis=1).reshape(
        heads_here, ctx_count, per_owner
    )
    counts_recv = lax.all_to_all(counts_send, "ctx", split_axis=1, concat_axis=1, tiled=True)
    stacked = jnp.concatenate(
        (
            query_rows.reshape(token_count, heads_here, head_dim),
            key_rows.reshape(token_count, heads_here, head_dim),
            value_rows.reshape(token_count, heads_here, head_dim),
        ),
        axis=2,
    )
    weight_view = out_weight.reshape(head_count, heads_here * head_dim, out_cols)
    slot_ids = jnp.arange(row_total, dtype=jnp.int32)
    mixed_total = None
    sums_parts, counts_parts = [], []
    first = 0
    for group_heads in sizes:
        heads = slice(first, first + group_heads)
        first += group_heads
        selector = (slot_ids[None, :, None] == targets[heads][:, None, :]).astype(jnp.bfloat16)
        send = jnp.einsum(
            "hrt,thd->hrd", selector, stacked[:, heads], preferred_element_type=jnp.float32
        ).astype(jnp.bfloat16)
        send = send.reshape(group_heads, ctx_count, slot_count * per_owner, 3 * head_dim)
        recv = lax.all_to_all(send, "ctx", split_axis=1, concat_axis=1, tiled=True)
        result, key_sums, key_counts = attend_blocks(recv, counts_recv[heads], per_owner, head_dim)
        sums_parts.append(key_sums)
        counts_parts.append(key_counts)
        returned = lax.all_to_all(result, "ctx", split_axis=1, concat_axis=1, tiled=True)
        returned = returned.reshape(group_heads, row_total, head_dim)
        attended = jnp.einsum(
            "hrt,hrd->thd", selector, returned, preferred_element_type=jnp.float32
        ).astype(jnp.bfloat16).reshape(token_count, group_heads * head_dim)
        gathered = lax.all_gather(attended, "head", axis=1, tiled=True)
        part = jnp.dot(
            gathered,
            weight_view[:, heads.start * head_dim : heads.stop * head_dim].reshape(
                head_count * group_heads * head_dim, out_cols
            ),
            preferred_element_type=jnp.float32,
        )
        mixed_total = part if mixed_total is None else mixed_total + part
    key_sums = jnp.concatenate(sums_parts, axis=0)
    key_counts = jnp.concatenate(counts_parts, axis=0)
    new_centroids = (prior_weight * centroids + key_sums) / (prior_weight + key_counts[:, :, None])
    return (mixed_total.astype(jnp.bfloat16), new_centroids)


def solution(mesh):
    placed = (
        P("ctx", "head"),
        P("ctx", "head"),
        P("ctx", "head"),
        P("head", "ctx", None),
        P("head", "ctx", None),
        P(None, "head"),
    )
    return jax.shard_map(
        local,
        mesh=mesh,
        in_specs=placed,
        out_specs=(P("ctx", "head"), P("head", "ctx", None)),
        check_vma=False,
    )
```

```python
import jax
import jax.numpy as jnp
from jax import lax
from jax.sharding import PartitionSpec as P

CLUSTERS = 256


prior_weight = 64.0


def slot_targets(labels, per_owner, slot_count):
    length = labels.shape[1]
    order_ids = jnp.arange(length, dtype=jnp.int32)
    same_label = labels[:, :, None] == labels[:, None, :]
    earlier = order_ids[None, :] < order_ids[:, None]
    token_rank = jnp.sum((same_label & earlier[None]).astype(jnp.int32), axis=2)
    owner_of = labels // per_owner
    local_of = labels % per_owner
    return owner_of * (slot_count * per_owner) + token_rank * per_owner + local_of


def attend_blocks(recv, counts_recv, per_owner, head_dim):
    heads_here, sources, width_slots, _ = recv.shape
    slot_count = width_slots // per_owner
    row_count = sources * slot_count
    view = recv.reshape(heads_here, row_count, per_owner, 3 * head_dim)
    query_view = view[..., :head_dim]
    key_view = view[..., head_dim : 2 * head_dim]
    value_view = view[..., 2 * head_dim :]
    rank_ids = jnp.arange(slot_count, dtype=jnp.int32)
    valid = rank_ids[None, None, :, None] < counts_recv[:, :, None, :]
    valid = jnp.transpose(valid.reshape(heads_here, row_count, per_owner), (0, 2, 1))
    row_ids = jnp.arange(row_count, dtype=jnp.int32)
    causal = row_ids[None, :] <= row_ids[:, None]
    allowed = valid[:, :, None, :] & causal[None, None]
    scores = jnp.einsum(
        "hicd,hjcd->hcij", query_view, key_view, preferred_element_type=jnp.float32
    ) * head_dim ** (-0.5)
    scores = jnp.where(allowed, scores, jnp.float32(-1e30))
    top_score = jnp.max(scores, axis=3, keepdims=True)
    weights = jnp.exp(scores - top_score)
    totals = jnp.sum(weights, axis=3, keepdims=True)
    attention_weights = (weights / totals).astype(jnp.bfloat16)
    result = jnp.einsum(
        "hcij,hjcd->hicd", attention_weights, value_view, preferred_element_type=jnp.float32
    ).astype(jnp.bfloat16)
    key_sums = jnp.sum(key_view.astype(jnp.float32), axis=1)
    key_counts = jnp.sum(counts_recv, axis=1).astype(jnp.float32)
    return result.reshape(heads_here, sources, width_slots, head_dim), key_sums, key_counts


GROUP_SIZES = (3, 3, 2)


def local(query_rows, key_rows, value_rows, cluster_ids, centroids, out_weight):
    ctx_count = lax.axis_size("ctx")
    head_count = lax.axis_size("head")
    token_count = query_rows.shape[0]
    heads_here = cluster_ids.shape[0]
    head_dim = query_rows.shape[1] // heads_here
    out_cols = out_weight.shape[1]
    clusters = CLUSTERS
    per_owner = clusters // ctx_count
    slot_count = 2 * token_count // clusters
    row_total = clusters * slot_count
    sizes = GROUP_SIZES if sum(GROUP_SIZES) == heads_here else (heads_here,)
    labels = cluster_ids[:, :, 0]
    targets = slot_targets(labels, per_owner, slot_count)
    one_hot = labels[:, :, None] == jnp.arange(clusters, dtype=jnp.int32)[None, None, :]
    counts_send = jnp.sum(one_hot.astype(jnp.int32), axis=1).reshape(
        heads_here, ctx_count, per_owner
    )
    counts_recv = lax.all_to_all(counts_send, "ctx", split_axis=1, concat_axis=1, tiled=True)
    weight_view = out_weight.reshape(head_count, heads_here * head_dim, out_cols)
    slot_ids = jnp.arange(row_total, dtype=jnp.int32)
    mixed_total = None
    sums_parts, counts_parts = [], []
    first = 0
    for group_heads in sizes:
        heads = slice(first, first + group_heads)
        first += group_heads
        selector = (slot_ids[None, :, None] == targets[heads][:, None, :]).astype(jnp.bfloat16)
        cols = slice(heads.start * head_dim, heads.stop * head_dim)
        stacked = jnp.concatenate(
            [
                rows[:, cols].reshape(token_count, group_heads, head_dim)
                for rows in (query_rows, key_rows, value_rows)
            ],
            axis=2,
        )
        send = jnp.einsum(
            "hrt,thd->hrd", selector, stacked, preferred_element_type=jnp.float32
        ).astype(jnp.bfloat16)
        send = send.reshape(group_heads, ctx_count, slot_count * per_owner, 3 * head_dim)
        recv = lax.all_to_all(send, "ctx", split_axis=1, concat_axis=1, tiled=True)
        result, key_sums, key_counts = attend_blocks(recv, counts_recv[heads], per_owner, head_dim)
        sums_parts.append(key_sums)
        counts_parts.append(key_counts)
        returned = lax.all_to_all(result, "ctx", split_axis=1, concat_axis=1, tiled=True)
        returned = returned.reshape(group_heads, row_total, head_dim)
        attended = jnp.einsum(
            "hrt,hrd->thd", selector, returned, preferred_element_type=jnp.float32
        ).astype(jnp.bfloat16).reshape(token_count, group_heads * head_dim)
        gathered = lax.all_gather(attended, "head", axis=1, tiled=True)
        part = jnp.dot(
            gathered,
            weight_view[:, heads.start * head_dim : heads.stop * head_dim].reshape(
                head_count * group_heads * head_dim, out_cols
            ),
            preferred_element_type=jnp.float32,
        )
        mixed_total = part if mixed_total is None else mixed_total + part
    key_sums = jnp.concatenate(sums_parts, axis=0)
    key_counts = jnp.concatenate(counts_parts, axis=0)
    new_centroids = (prior_weight * centroids + key_sums) / (prior_weight + key_counts[:, :, None])
    return (mixed_total.astype(jnp.bfloat16), new_centroids)


def solution(mesh):
    placed = (
        P("ctx", "head"),
        P("ctx", "head"),
        P("ctx", "head"),
        P("head", "ctx", None),
        P("head", "ctx", None),
        P(None, "head"),
    )
    return jax.shard_map(
        local,
        mesh=mesh,
        in_specs=placed,
        out_specs=(P("ctx", "head"), P("head", "ctx", None)),
        check_vma=False,
    )
```

```python
import jax
import jax.numpy as jnp
from jax import lax
from jax.sharding import PartitionSpec as P

CLUSTERS = 256


prior_weight = 64.0


def slot_targets(labels, per_owner, slot_count):
    length = labels.shape[1]
    order_ids = jnp.arange(length, dtype=jnp.int32)
    same_label = labels[:, :, None] == labels[:, None, :]
    earlier = order_ids[None, :] < order_ids[:, None]
    token_rank = jnp.sum((same_label & earlier[None]).astype(jnp.int32), axis=2)
    owner_of = labels // per_owner
    local_of = labels % per_owner
    return owner_of * (slot_count * per_owner) + token_rank * per_owner + local_of


def attend_blocks(recv, counts_recv, per_owner, head_dim):
    heads_here, sources, width_slots, _ = recv.shape
    slot_count = width_slots // per_owner
    row_count = sources * slot_count
    view = recv.reshape(heads_here, row_count, per_owner, 3 * head_dim)
    query_view = view[..., :head_dim]
    key_view = view[..., head_dim : 2 * head_dim]
    value_view = view[..., 2 * head_dim :]
    rank_ids = jnp.arange(slot_count, dtype=jnp.int32)
    valid = rank_ids[None, None, :, None] < counts_recv[:, :, None, :]
    valid = jnp.transpose(valid.reshape(heads_here, row_count, per_owner), (0, 2, 1))
    row_ids = jnp.arange(row_count, dtype=jnp.int32)
    causal = row_ids[None, :] <= row_ids[:, None]
    allowed = valid[:, :, None, :] & causal[None, None]
    scores = jnp.einsum(
        "hicd,hjcd->hcij", query_view, key_view, preferred_element_type=jnp.float32
    ) * head_dim ** (-0.5)
    scores = jnp.where(allowed, scores, jnp.float32(-1e30))
    top_score = jnp.max(scores, axis=3, keepdims=True)
    weights = jnp.exp(scores - top_score)
    totals = jnp.sum(weights, axis=3, keepdims=True)
    attention_weights = (weights / totals).astype(jnp.bfloat16)
    result = jnp.einsum(
        "hcij,hjcd->hicd", attention_weights, value_view, preferred_element_type=jnp.float32
    ).astype(jnp.bfloat16)
    key_sums = jnp.sum(key_view.astype(jnp.float32), axis=1)
    key_counts = jnp.sum(counts_recv, axis=1).astype(jnp.float32)
    return result.reshape(heads_here, sources, width_slots, head_dim), key_sums, key_counts


GROUP_SIZES = (3, 3, 2)


def local(query_rows, key_rows, value_rows, cluster_ids, centroids, out_weight):
    ctx_count = lax.axis_size("ctx")
    head_count = lax.axis_size("head")
    token_count = query_rows.shape[0]
    heads_here = cluster_ids.shape[0]
    head_dim = query_rows.shape[1] // heads_here
    out_cols = out_weight.shape[1]
    clusters = CLUSTERS
    per_owner = clusters // ctx_count
    slot_count = 2 * token_count // clusters
    row_total = clusters * slot_count
    sizes = GROUP_SIZES if sum(GROUP_SIZES) == heads_here else (heads_here,)
    labels = cluster_ids[:, :, 0]
    one_hot = labels[:, :, None] == jnp.arange(clusters, dtype=jnp.int32)[None, None, :]
    counts_send = jnp.sum(one_hot.astype(jnp.int32), axis=1).reshape(
        heads_here, ctx_count, per_owner
    )
    counts_recv = lax.all_to_all(counts_send, "ctx", split_axis=1, concat_axis=1, tiled=True)
    weight_view = out_weight.reshape(head_count, heads_here * head_dim, out_cols)
    slot_ids = jnp.arange(row_total, dtype=jnp.int32)
    mixed_total = None
    sums_parts, counts_parts = [], []
    first = 0
    for group_heads in sizes:
        heads = slice(first, first + group_heads)
        first += group_heads
        group_targets = slot_targets(labels[heads], per_owner, slot_count)
        selector = (slot_ids[None, :, None] == group_targets[:, None, :]).astype(jnp.bfloat16)
        cols = slice(heads.start * head_dim, heads.stop * head_dim)
        stacked = jnp.concatenate(
            [
                rows[:, cols].reshape(token_count, group_heads, head_dim)
                for rows in (query_rows, key_rows, value_rows)
            ],
            axis=2,
        )
        send = jnp.einsum(
            "hrt,thd->hrd", selector, stacked, preferred_element_type=jnp.float32
        ).astype(jnp.bfloat16)
        send = send.reshape(group_heads, ctx_count, slot_count * per_owner, 3 * head_dim)
        recv = lax.all_to_all(send, "ctx", split_axis=1, concat_axis=1, tiled=True)
        result, key_sums, key_counts = attend_blocks(recv, counts_recv[heads], per_owner, head_dim)
        sums_parts.append(key_sums)
        counts_parts.append(key_counts)
        returned = lax.all_to_all(result, "ctx", split_axis=1, concat_axis=1, tiled=True)
        returned = returned.reshape(group_heads, row_total, head_dim)
        attended = jnp.einsum(
            "hrt,hrd->thd", selector, returned, preferred_element_type=jnp.float32
        ).astype(jnp.bfloat16).reshape(token_count, group_heads * head_dim)
        gathered = lax.all_gather(attended, "head", axis=1, tiled=True)
        part = jnp.dot(
            gathered,
            weight_view[:, heads.start * head_dim : heads.stop * head_dim].reshape(
                head_count * group_heads * head_dim, out_cols
            ),
            preferred_element_type=jnp.float32,
        )
        mixed_total = part if mixed_total is None else mixed_total + part
    key_sums = jnp.concatenate(sums_parts, axis=0)
    key_counts = jnp.concatenate(counts_parts, axis=0)
    new_centroids = (prior_weight * centroids + key_sums) / (prior_weight + key_counts[:, :, None])
    return (mixed_total.astype(jnp.bfloat16), new_centroids)


def solution(mesh):
    placed = (
        P("ctx", "head"),
        P("ctx", "head"),
        P("ctx", "head"),
        P("head", "ctx", None),
        P("head", "ctx", None),
        P(None, "head"),
    )
    return jax.shard_map(
        local,
        mesh=mesh,
        in_specs=placed,
        out_specs=(P("ctx", "head"), P("head", "ctx", None)),
        check_vma=False,
    )
```

```python
import jax
import jax.numpy as jnp
from jax import lax
from jax.sharding import PartitionSpec as P

CLUSTERS = 256


prior_weight = 64.0


def slot_targets(labels, per_owner, slot_count):
    length = labels.shape[1]
    order_ids = jnp.arange(length, dtype=jnp.int32)
    same_label = labels[:, :, None] == labels[:, None, :]
    earlier = order_ids[None, :] < order_ids[:, None]
    token_rank = jnp.sum((same_label & earlier[None]).astype(jnp.int32), axis=2)
    owner_of = labels // per_owner
    local_of = labels % per_owner
    return owner_of * (slot_count * per_owner) + token_rank * per_owner + local_of


def attend_blocks(recv, counts_recv, per_owner, head_dim):
    heads_here, sources, width_slots, _ = recv.shape
    slot_count = width_slots // per_owner
    row_count = sources * slot_count
    view = recv.reshape(heads_here, row_count, per_owner, 3 * head_dim)
    query_view = view[..., :head_dim]
    key_view = view[..., head_dim : 2 * head_dim]
    value_view = view[..., 2 * head_dim :]
    rank_ids = jnp.arange(slot_count, dtype=jnp.int32)
    valid = rank_ids[None, None, :, None] < counts_recv[:, :, None, :]
    valid = jnp.transpose(valid.reshape(heads_here, row_count, per_owner), (0, 2, 1))
    row_ids = jnp.arange(row_count, dtype=jnp.int32)
    causal = row_ids[None, :] <= row_ids[:, None]
    allowed = valid[:, :, None, :] & causal[None, None]
    scores = jnp.einsum(
        "hicd,hjcd->hcij", query_view, key_view, preferred_element_type=jnp.float32
    ) * head_dim ** (-0.5)
    scores = jnp.where(allowed, scores, jnp.float32(-1e30))
    top_score = jnp.max(scores, axis=3, keepdims=True)
    weights = jnp.exp(scores - top_score)
    totals = jnp.sum(weights, axis=3, keepdims=True)
    attention_weights = (weights / totals).astype(jnp.bfloat16)
    result = jnp.einsum(
        "hcij,hjcd->hicd", attention_weights, value_view, preferred_element_type=jnp.float32
    ).astype(jnp.bfloat16)
    key_sums = jnp.sum(key_view.astype(jnp.float32), axis=1)
    key_counts = jnp.sum(counts_recv, axis=1).astype(jnp.float32)
    return result.reshape(heads_here, sources, width_slots, head_dim), key_sums, key_counts


GROUP_SIZES = (2, 3, 3)


def local(query_rows, key_rows, value_rows, cluster_ids, centroids, out_weight):
    ctx_count = lax.axis_size("ctx")
    head_count = lax.axis_size("head")
    token_count = query_rows.shape[0]
    heads_here = cluster_ids.shape[0]
    head_dim = query_rows.shape[1] // heads_here
    out_cols = out_weight.shape[1]
    clusters = CLUSTERS
    per_owner = clusters // ctx_count
    slot_count = 2 * token_count // clusters
    row_total = clusters * slot_count
    sizes = GROUP_SIZES if sum(GROUP_SIZES) == heads_here else (heads_here,)
    labels = cluster_ids[:, :, 0]
    one_hot = labels[:, :, None] == jnp.arange(clusters, dtype=jnp.int32)[None, None, :]
    counts_send = jnp.sum(one_hot.astype(jnp.int32), axis=1).reshape(
        heads_here, ctx_count, per_owner
    )
    counts_rows = jnp.transpose(counts_send, (1, 0, 2)).reshape(ctx_count, heads_here * per_owner)
    counts_recv = None
    weight_view = out_weight.reshape(head_count, heads_here * head_dim, out_cols)
    slot_ids = jnp.arange(row_total, dtype=jnp.int32)
    mixed_total = None
    sums_parts, counts_parts = [], []
    first = 0
    for group_heads in sizes:
        heads = slice(first, first + group_heads)
        first += group_heads
        group_targets = slot_targets(labels[heads], per_owner, slot_count)
        selector = (slot_ids[None, :, None] == group_targets[:, None, :]).astype(jnp.bfloat16)
        cols = slice(heads.start * head_dim, heads.stop * head_dim)
        stacked = jnp.concatenate(
            [
                rows[:, cols].reshape(token_count, group_heads, head_dim)
                for rows in (query_rows, key_rows, value_rows)
            ],
            axis=2,
        )
        send = jnp.einsum(
            "hrt,thd->hrd", selector, stacked, preferred_element_type=jnp.float32
        ).astype(jnp.bfloat16)
        send = send.reshape(group_heads, ctx_count, slot_count * per_owner, 3 * head_dim)
        carries = counts_recv is None and heads_here * per_owner <= 3 * head_dim
        if carries:
            extra = jnp.zeros((group_heads, ctx_count, 16, 3 * head_dim), jnp.bfloat16)
            extra = extra.at[0, :, 0, : heads_here * per_owner].set(counts_rows.astype(jnp.bfloat16))
            send = jnp.concatenate((send, extra), axis=2)
        elif counts_recv is None:
            counts_recv = lax.all_to_all(
                counts_send, "ctx", split_axis=1, concat_axis=1, tiled=True
            )
        recv = lax.all_to_all(send, "ctx", split_axis=1, concat_axis=1, tiled=True)
        if carries:
            counts_recv = jnp.transpose(
                recv[0, :, slot_count * per_owner, : heads_here * per_owner]
                .astype(jnp.int32)
                .reshape(ctx_count, heads_here, per_owner),
                (1, 0, 2),
            )
            recv = recv[:, :, : slot_count * per_owner]
        result, key_sums, key_counts = attend_blocks(recv, counts_recv[heads], per_owner, head_dim)
        sums_parts.append(key_sums)
        counts_parts.append(key_counts)
        returned = lax.all_to_all(result, "ctx", split_axis=1, concat_axis=1, tiled=True)
        returned = returned.reshape(group_heads, row_total, head_dim)
        attended = jnp.einsum(
            "hrt,hrd->thd", selector, returned, preferred_element_type=jnp.float32
        ).astype(jnp.bfloat16).reshape(token_count, group_heads * head_dim)
        gathered = lax.all_gather(attended, "head", axis=1, tiled=True)
        part = jnp.dot(
            gathered,
            weight_view[:, heads.start * head_dim : heads.stop * head_dim].reshape(
                head_count * group_heads * head_dim, out_cols
            ),
            preferred_element_type=jnp.float32,
        )
        mixed_total = part if mixed_total is None else mixed_total + part
    key_sums = jnp.concatenate(sums_parts, axis=0)
    key_counts = jnp.concatenate(counts_parts, axis=0)
    new_centroids = (prior_weight * centroids + key_sums) / (prior_weight + key_counts[:, :, None])
    return (mixed_total.astype(jnp.bfloat16), new_centroids)


def solution(mesh):
    placed = (
        P("ctx", "head"),
        P("ctx", "head"),
        P("ctx", "head"),
        P("head", "ctx", None),
        P("head", "ctx", None),
        P(None, "head"),
    )
    return jax.shard_map(
        local,
        mesh=mesh,
        in_specs=placed,
        out_specs=(P("ctx", "head"), P("head", "ctx", None)),
        check_vma=False,
    )
```

```python
import jax
import jax.numpy as jnp
from jax import lax
from jax.sharding import PartitionSpec as P

CLUSTERS = 256


prior_weight = 64.0


def slot_targets(labels, per_owner, slot_count):
    length = labels.shape[1]
    order_ids = jnp.arange(length, dtype=jnp.int32)
    same_label = labels[:, :, None] == labels[:, None, :]
    earlier = order_ids[None, :] < order_ids[:, None]
    token_rank = jnp.sum((same_label & earlier[None]).astype(jnp.int32), axis=2)
    owner_of = labels // per_owner
    local_of = labels % per_owner
    return owner_of * (slot_count * per_owner) + token_rank * per_owner + local_of


def attend_blocks(recv, counts_recv, per_owner, head_dim):
    heads_here, sources, width_slots, _ = recv.shape
    slot_count = width_slots // per_owner
    row_count = sources * slot_count
    view = recv.reshape(heads_here, row_count, per_owner, 3 * head_dim)
    query_view = view[..., :head_dim]
    key_view = view[..., head_dim : 2 * head_dim]
    value_view = view[..., 2 * head_dim :]
    rank_ids = jnp.arange(slot_count, dtype=jnp.int32)
    valid = rank_ids[None, None, :, None] < counts_recv[:, :, None, :]
    valid = jnp.transpose(valid.reshape(heads_here, row_count, per_owner), (0, 2, 1))
    row_ids = jnp.arange(row_count, dtype=jnp.int32)
    causal = row_ids[None, :] <= row_ids[:, None]
    allowed = valid[:, :, None, :] & causal[None, None]
    scores = jnp.einsum(
        "hicd,hjcd->hcij", query_view, key_view, preferred_element_type=jnp.float32
    ) * head_dim ** (-0.5)
    scores = jnp.where(allowed, scores, jnp.float32(-1e30))
    top_score = jnp.max(scores, axis=3, keepdims=True)
    weights = jnp.exp(scores - top_score)
    totals = jnp.sum(weights, axis=3, keepdims=True)
    attention_weights = (weights / totals).astype(jnp.bfloat16)
    result = jnp.einsum(
        "hcij,hjcd->hicd", attention_weights, value_view, preferred_element_type=jnp.float32
    ).astype(jnp.bfloat16)
    key_sums = jnp.sum(key_view.astype(jnp.float32), axis=1)
    key_counts = jnp.sum(counts_recv, axis=1).astype(jnp.float32)
    return result.reshape(heads_here, sources, width_slots, head_dim), key_sums, key_counts


GROUP_SIZES = (2, 3, 3)


def local(query_rows, key_rows, value_rows, cluster_ids, centroids, out_weight):
    ctx_count = lax.axis_size("ctx")
    head_count = lax.axis_size("head")
    token_count = query_rows.shape[0]
    heads_here = cluster_ids.shape[0]
    head_dim = query_rows.shape[1] // heads_here
    out_cols = out_weight.shape[1]
    clusters = CLUSTERS
    per_owner = clusters // ctx_count
    slot_count = 2 * token_count // clusters
    row_total = clusters * slot_count
    sizes = GROUP_SIZES if sum(GROUP_SIZES) == heads_here else (heads_here,)
    labels = cluster_ids[:, :, 0]
    one_hot = labels[:, :, None] == jnp.arange(clusters, dtype=jnp.int32)[None, None, :]
    counts_send = jnp.sum(one_hot.astype(jnp.int32), axis=1).reshape(
        heads_here, ctx_count, per_owner
    )
    counts_rows = jnp.transpose(counts_send, (1, 0, 2)).reshape(ctx_count, heads_here * per_owner)
    counts_recv = None
    weight_view = out_weight.reshape(head_count, heads_here * head_dim, out_cols)
    slot_ids = jnp.arange(row_total, dtype=jnp.int32)
    mixed_total = None
    sums_parts, counts_parts = [], []
    first = 0
    group_weights = None
    for group_heads in sizes:
        heads = slice(first, first + group_heads)
        first += group_heads
        group_targets = slot_targets(labels[heads], per_owner, slot_count)
        selector = (slot_ids[None, :, None] == group_targets[:, None, :]).astype(jnp.bfloat16)
        cols = slice(heads.start * head_dim, heads.stop * head_dim)
        stacked = jnp.concatenate(
            [
                rows[:, cols].reshape(token_count, group_heads, head_dim)
                for rows in (query_rows, key_rows, value_rows)
            ],
            axis=2,
        )
        send = jnp.einsum(
            "hrt,thd->hrd", selector, stacked, preferred_element_type=jnp.float32
        ).astype(jnp.bfloat16)
        send = send.reshape(group_heads, ctx_count, slot_count * per_owner, 3 * head_dim)
        carries = counts_recv is None and heads_here * per_owner <= 3 * head_dim
        if carries:
            extra = jnp.zeros((group_heads, ctx_count, 16, 3 * head_dim), jnp.bfloat16)
            extra = extra.at[0, :, 0, : heads_here * per_owner].set(counts_rows.astype(jnp.bfloat16))
            send = jnp.concatenate((send, extra), axis=2)
        elif counts_recv is None:
            counts_recv = lax.all_to_all(
                counts_send, "ctx", split_axis=1, concat_axis=1, tiled=True
            )
        recv = lax.all_to_all(send, "ctx", split_axis=1, concat_axis=1, tiled=True)
        if group_weights is None:
            spans, start = [], 0
            for size in sizes:
                spans.append(
                    weight_view[:, start * head_dim : (start + size) * head_dim].reshape(
                        head_count * size * head_dim, out_cols
                    )
                )
                start += size
            group_weights, recv = lax.optimization_barrier((spans, recv))
        if carries:
            counts_recv = jnp.transpose(
                recv[0, :, slot_count * per_owner, : heads_here * per_owner]
                .astype(jnp.int32)
                .reshape(ctx_count, heads_here, per_owner),
                (1, 0, 2),
            )
            recv = recv[:, :, : slot_count * per_owner]
        result, key_sums, key_counts = attend_blocks(recv, counts_recv[heads], per_owner, head_dim)
        sums_parts.append(key_sums)
        counts_parts.append(key_counts)
        returned = lax.all_to_all(result, "ctx", split_axis=1, concat_axis=1, tiled=True)
        returned = returned.reshape(group_heads, row_total, head_dim)
        attended = jnp.einsum(
            "hrt,hrd->thd", selector, returned, preferred_element_type=jnp.float32
        ).astype(jnp.bfloat16).reshape(token_count, group_heads * head_dim)
        gathered = lax.all_gather(attended, "head", axis=1, tiled=True)
        part = jnp.dot(
            gathered, group_weights[len(sums_parts) - 1], preferred_element_type=jnp.float32
        )
        mixed_total = part if mixed_total is None else mixed_total + part
    key_sums = jnp.concatenate(sums_parts, axis=0)
    key_counts = jnp.concatenate(counts_parts, axis=0)
    new_centroids = (prior_weight * centroids + key_sums) / (prior_weight + key_counts[:, :, None])
    return (mixed_total.astype(jnp.bfloat16), new_centroids)


def solution(mesh):
    placed = (
        P("ctx", "head"),
        P("ctx", "head"),
        P("ctx", "head"),
        P("head", "ctx", None),
        P("head", "ctx", None),
        P(None, "head"),
    )
    return jax.shard_map(
        local,
        mesh=mesh,
        in_specs=placed,
        out_specs=(P("ctx", "head"), P("head", "ctx", None)),
        check_vma=False,
    )
```
